256 devices in a mesh: grp: 32 (over y, z_lo, core), tp: 8 (over x, z_hi).
Axes of the slice: x: 4, y: 4, z: 8 (z_hi: 2, z_lo: 4; z = z_hi * 4 + z_lo), core: 2. Of those that a mesh axis runs over, the one named last changes fastest.
Arguments:
- tok_ids: int32 [8192], P('grp'), may hold values from 0 to 16383
- accept: int32 [8192], P('grp'), may hold values 0 or 1
- sub_ids: int32 [8192], P('grp'), may hold values from 0 to 16383
- cache_len: int32 [32], replicated, may hold values from 256 to 3840, as said below
- spill: int32 [32], replicated, may hold values from 0 to 1792, as said below
- embed: bfloat16 [16384, 2048], P('grp', 'tp'), may hold values from -6 to 6
- attn_gain: float32 [2048], replicated, may hold values from 0.25 to 1.75
- w_query: bfloat16 [2048, 2048], P(None, 'tp'), may hold values from -0.125 to 0.125
- w_key: bfloat16 [2048, 512], P(None, 'tp'), as said below
- w_value: bfloat16 [2048, 512], P(None, 'tp'), as said below
- w_out: bfloat16 [2048, 2048], P('tp'), may hold values from -2.5 to 2.5
- mlp_gain: float32 [2048], replicated, may hold values from 0.25 to 1.75
- w_gate: bfloat16 [2048, 5632], P(None, 'tp'), may hold values from -0.125 to 0.125
- w_up: bfloat16 [2048, 5632], P(None, 'tp'), may hold values from -0.125 to 0.125
- w_down: bfloat16 [5632, 2048], P('tp'), may hold values from -0.078125 to 0.078125
- cache_keys: bfloat16 [65536, 512], P('grp', 'tp'), may hold values from -320 to 320, as said below
- cache_values: bfloat16 [65536, 512], P('grp', 'tp'), may hold values from -8 to 8, as said below
Outputs:
- first_out: bfloat16 [8192, 2048], P('grp', 'tp')
- second_out: bfloat16 [8192, 2048], P('grp', 'tp')
The draws below stay inside these ranges and needn't reach their ends.
Inputs may be any that keep to these rules, and one draw needn't show every extreme that they name: Request g keeps cache_len[g] - spill[g] >= 256 positions in slots from 0 of store g and spill[g] positions in the last slots of store (g xor 1); for every g, cache_len[g] - spill[g] + spill[g xor 1] <= 2048. Of each pair of groups 2k, 2k + 1 at most one has spill above 0. `w_key`: the 2 stored copies of a key-value head are equal. `w_value`: the 2 stored copies of a key-value head are equal. `cache_keys`: the 2 stored copies of a key-value head are equal. `cache_values`: the 2 stored copies of a key-value head are equal.
All inputs are finite; a program needn't handle non-finite values. No bound on the sum of `accept` on one device may be relied on, other than what follows from the above.
Results may differ from the reference program's by a relative error of at most 0.024.
Values may be sent and summed in bfloat16 or wider, within the bound.
No kernel may reach another device: no remote copies, remote signals or barrier semaphores. Data moves between devices by JAX's collectives and lax.ppermute only.
A program may use at most 128 MiB of HBM per device.

```python
import math
import jax
import jax.numpy as jnp
import numpy as np
from jax import lax

D = 2048
QH = 32
KVH = 4
HD = 64
FF = 5632
VOCAB = 16384
BLOCK = 256
SLOTS = 2048
KVC = 8
TOKENS = 8192
N_GRP = 32
N_TP = 8


def pair_layout(key):
    pairs = N_GRP // 2
    keys = jax.random.split(jax.random.fold_in(key, 7), 5)
    is_long = jax.random.randint(keys[0], (pairs,), 0, 2)
    is_long = is_long.at[0].set(1).at[1].set(0)
    which = jax.random.randint(keys[1], (pairs,), 0, 2)
    long_len = jax.random.randint(keys[2], (pairs,), SLOTS + BLOCK, 2 * SLOTS - BLOCK + 1)
    long_len = long_len.at[0].set(2 * SLOTS - BLOCK)
    other_len = jax.random.randint(keys[3], (pairs,), BLOCK, 2 * SLOTS - long_len + 1)
    short_len = jax.random.randint(keys[4], (pairs, 2), BLOCK, SLOTS + 1)
    long_pair = is_long == 1
    len_first = jnp.where(long_pair, jnp.where(which == 0, long_len, other_len), short_len[:, 0])
    len_second = jnp.where(long_pair, jnp.where(which == 1, long_len, other_len), short_len[:, 1])
    spill_first = jnp.where(long_pair & (which == 0), long_len - SLOTS, 0)
    spill_second = jnp.where(long_pair & (which == 1), long_len - SLOTS, 0)
    lengths = jnp.stack([len_first, len_second], axis=1).reshape(N_GRP)
    spills = jnp.stack([spill_first, spill_second], axis=1).reshape(N_GRP)
    return (lengths.astype(jnp.int32), spills.astype(jnp.int32))


def draw_cache_len(key, part):
    return pair_layout(key)[0]


def draw_spill(key, part):
    return pair_layout(key)[1]


def repeated_weight(key, salt):
    base = jax.random.truncated_normal(jax.random.fold_in(key, salt), -6.0, 6.0, (D, KVH, HD), jnp.float32) * D ** (-0.5)
    full = jnp.repeat(base, KVC // KVH, axis=1)
    return full.reshape(D, KVC * HD).astype(jnp.bfloat16)


def draw_w_key(key, part):
    return repeated_weight(key, 31)


def draw_w_value(key, part):
    return repeated_weight(key, 32)


def draw_cache_keys(key, part):
    parts = jax.random.split(jax.random.fold_in(key, 21), 2)
    shape = (N_GRP, SLOTS, KVH, HD)
    full = jax.random.truncated_normal(parts[1], -6.0, 6.0, shape, jnp.float32)
    full = jnp.repeat(full, KVC // KVH, axis=2)
    return full.reshape(N_GRP * SLOTS, KVC * HD).astype(jnp.bfloat16)


def draw_cache_values(key, part):
    parts = jax.random.split(jax.random.fold_in(key, 22), 2)
    shape = (N_GRP, SLOTS, KVH, HD)
    full = jax.random.truncated_normal(parts[1], -6.0, 6.0, shape, jnp.float32)
    full = jnp.repeat(full, KVC // KVH, axis=2)
    return full.reshape(N_GRP * SLOTS, KVC * HD).astype(jnp.bfloat16)


def with_ends(result, own_key, least, top_value):
    spot = [jax.random.randint(jax.random.fold_in(own_key, axis), (), 0, length) for axis, length in enumerate(result.shape)]
    widest = result.shape.index(max(result.shape))
    neighbour = spot[:widest] + [(spot[widest] + 1) % result.shape[widest]] + spot[widest + 1:]
    return result.at[tuple(spot)].set(least).at[tuple(neighbour)].set(top_value)


def shard_levels(key, extent, cuts, low, largest):
    loudness = 1.0
    for dim, blocks in cuts:
        heights = jax.random.uniform(jax.random.fold_in(jax.random.fold_in(key, 6), dim), (blocks,), jnp.float32, low / len(cuts), largest / len(cuts))
        loudness = loudness * jnp.repeat(jnp.exp(heights), extent[dim] // blocks).reshape((-1,) + (1,) * (len(extent) - 1 - dim))
    return loudness


def cumulative_ranks(amount, lean):
    weights = [(1 << 20) // math.isqrt(rank ** lean) + 1 for rank in range(1, amount + 1)]
    spread = 1 + sum(weights) // (1 << 30)
    return np.cumsum(np.array([max(1, weight // spread) for weight in weights]))


def ranked(key, dims, number_of, skew):
    grid = cumulative_ranks(number_of, skew)
    ticket = jax.random.randint(jax.random.fold_in(key, 1), dims, 0, int(grid[number_of - 1]))
    grade = jnp.searchsorted(jnp.asarray(grid, jnp.int32), ticket, side="right")
    return jax.random.permutation(jax.random.fold_in(key, 2), number_of)[grade].astype(jnp.int32)


def scatter_about(stream_key, shape, spread, reach, shards=(), kind=jnp.bfloat16):
    loudness = shard_levels(stream_key, shape, shards, -0.22, 0.18) if shards else 1.0
    values = jax.random.normal(stream_key, shape, jnp.float32) * spread * loudness
    return jnp.minimum(jnp.maximum(values, -reach), reach).astype(kind)


def setup_inputs(seed: int = 0) -> dict:
    splits = jax.random.split(jax.random.key(seed), 18)
    return {
        "tok_ids": with_ends(ranked(splits[0], (TOKENS,), VOCAB, 2), jax.random.fold_in(splits[0], 3), 0, VOCAB - 1).astype(jnp.int32),
        "accept": with_ends((jax.random.randint(splits[1], (TOKENS,), 0, 2) < 1).astype(jnp.int32), jax.random.fold_in(splits[1], 1), 0, 1),
        "sub_ids": with_ends(ranked(splits[2], (TOKENS,), VOCAB, 2), jax.random.fold_in(splits[2], 3), 0, VOCAB - 1).astype(jnp.int32),
        "cache_len": draw_cache_len(jax.random.fold_in(splits[17], 71), 0),
        "spill": draw_spill(jax.random.fold_in(splits[17], 71), 0),
        "embed": scatter_about(splits[5], (VOCAB, D), 1.0, 6.0, ((0, 32), (1, 8))),
        "attn_gain": jnp.clip(1.0 + 0.15 * jax.random.normal(splits[6], (D,), jnp.float32), 0.25, 1.75),
        "w_query": scatter_about(splits[7], (D, QH * HD), D ** -0.5, 0.125, ((1, 8),)),
        "w_key": draw_w_key(jax.random.fold_in(splits[17], 71), 0),
        "w_value": draw_w_value(jax.random.fold_in(splits[17], 71), 0),
        "w_out": scatter_about(splits[10], (QH * HD, D), (8.0 / (QH * HD) ** 0.5), 2.5, ((0, 8),)),
        "mlp_gain": jnp.clip(1.0 + 0.15 * jax.random.normal(splits[11], (D,), jnp.float32), 0.25, 1.75),
        "w_gate": scatter_about(splits[12], (D, FF), D ** -0.5, 0.125, ((1, 8),)),
        "w_up": scatter_about(splits[13], (D, FF), D ** -0.5, 0.125, ((1, 8),)),
        "w_down": scatter_about(splits[14], (FF, D), FF ** -0.5, 0.078125, ((0, 8),)),
        "cache_keys": draw_cache_keys(jax.random.fold_in(splits[17], 71), 0),
        "cache_values": draw_cache_values(jax.random.fold_in(splits[17], 71), 0),
    }


def rms_normed(values, gain):
    square = lax.optimization_barrier(jnp.mean(values * values, axis=-1, keepdims=True))
    return (values * lax.rsqrt(square + 1e-05) * gain.astype(jnp.float32)).astype(jnp.bfloat16)

def rotate(vectors, positions):
    half = vectors.shape[-1] // 2
    exponent = jnp.arange(half, dtype=jnp.float32) * (-2.0 / vectors.shape[-1])
    freqs = jnp.power(jnp.float32(10000.0), exponent)
    angles = positions.astype(jnp.float32)[:, None] * freqs[None, :]
    cosine = jnp.cos(angles)[:, None, :]
    sine = jnp.sin(angles)[:, None, :]
    first = vectors[..., :half]
    second = vectors[..., half:]
    return jnp.concatenate([first * cosine - second * sine, second * cosine + first * sine], axis=-1)

def shard_sum(left, right):
    pieces = jnp.einsum('bti,tid->tbd', left.reshape(left.shape[0], N_TP, -1).astype(jnp.float32), right.reshape(N_TP, -1, right.shape[1]).astype(jnp.float32))
    rounded = lax.optimization_barrier(pieces.astype(jnp.bfloat16))
    return lax.optimization_barrier(jnp.sum(rounded.astype(jnp.float32), axis=0))

def reference(tok_ids, accept, sub_ids, cache_len, spill, embed, attn_gain, w_query, w_key, w_value, w_out, mlp_gain, w_gate, w_up, w_down, cache_keys, cache_values):
    second_ids = jnp.where(accept == 1, sub_ids, tok_ids)
    first_input = jnp.take(embed, tok_ids, axis=0)
    second_input = jnp.take(embed, second_ids, axis=0)
    stores_k = cache_keys.reshape(N_GRP, SLOTS, KVC, HD)
    stores_v = cache_values.reshape(N_GRP, SLOTS, KVC, HD)
    partner = jnp.bitwise_xor(jnp.arange(N_GRP, dtype=jnp.int32), 1)
    far_k = stores_k[partner]
    far_v = stores_v[partner]
    own_count = cache_len - spill

    def request_layer(packed):
        block_in, own_keys, own_values, far_keys, far_values, own_n, far_n, start = packed
        positions = start + jnp.arange(BLOCK, dtype=jnp.int32)
        normed = rms_normed(block_in.astype(jnp.float32), attn_gain)
        query = rotate(jnp.dot(normed, w_query, preferred_element_type=jnp.float32).reshape(BLOCK, QH, HD), positions)
        query = query.astype(jnp.bfloat16).reshape(BLOCK, KVC, QH // KVC, HD)
        new_keys = rotate(jnp.dot(normed, w_key, preferred_element_type=jnp.float32).reshape(BLOCK, KVC, HD), positions).astype(jnp.bfloat16)
        new_values = jnp.dot(normed, w_value, preferred_element_type=jnp.float32).reshape(BLOCK, KVC, HD).astype(jnp.bfloat16)
        slot_ids = jnp.arange(SLOTS, dtype=jnp.int32)
        valid = jnp.concatenate([slot_ids < own_n, slot_ids >= SLOTS - far_n, jnp.ones((BLOCK,), dtype=bool)])
        keys = jnp.concatenate([own_keys, far_keys, new_keys], axis=0)
        values = jnp.concatenate([own_values, far_values, new_values], axis=0)
        scores = jnp.einsum('bcgd,kcd->bcgk', query.astype(jnp.float32), keys.astype(jnp.float32)) * 0.125
        scores = jnp.where(valid, scores, -jnp.inf)
        top = lax.optimization_barrier(jnp.max(scores, axis=-1, keepdims=True))
        weights = jnp.exp(scores - top)
        total = lax.optimization_barrier(jnp.sum(weights, axis=-1, keepdims=True))
        probs = lax.optimization_barrier(weights.astype(jnp.bfloat16)).astype(jnp.float32)
        attended = jnp.einsum('bcgk,kcd->bcgd', probs, values.astype(jnp.float32)) / total
        mixed = attended.reshape(BLOCK, QH * HD).astype(jnp.bfloat16)
        head_sum = shard_sum(mixed, w_out)
        resid = (block_in.astype(jnp.float32) + head_sum).astype(jnp.bfloat16)
        normed_mlp = rms_normed(resid.astype(jnp.float32), mlp_gain)
        gate = jnp.dot(normed_mlp, w_gate, preferred_element_type=jnp.float32)
        lift = jnp.dot(normed_mlp, w_up, preferred_element_type=jnp.float32)
        hidden = (jax.nn.silu(gate) * lift).astype(jnp.bfloat16)
        mlp_sum = shard_sum(hidden, w_down)
        return (resid.astype(jnp.float32) + mlp_sum).astype(jnp.bfloat16)

    def one_pass(inputs):
        blocks = inputs.reshape(N_GRP, BLOCK, D)
        outputs = lax.map(request_layer, (blocks, stores_k, stores_v, far_k, far_v, own_count, spill, cache_len))
        return outputs.reshape(N_GRP * BLOCK, D)
    return (one_pass(first_input), one_pass(second_input))
```

```python
import jax
import jax.numpy as jnp
from jax import lax
from jax.sharding import PartitionSpec as P

HD = 64


EPSILON = 1e-05
SENTINEL = -1e30


def shifted(array, axis, step):
    n = lax.axis_size(axis)
    return lax.ppermute(array, axis, [(i, (i + step) % n) for i in range(n)])


def swapped(array, axis, bit):
    return lax.ppermute(array, axis, [(i, i ^ 1 << bit) for i in range(lax.axis_size(axis))])


def tp_gather(part):
    rows, width = part.shape
    n_x = lax.axis_size("tp") // 2
    me = lax.axis_index("tp")
    mine_x = me // 2
    partner = swapped(part, "tp", 0)
    low_first = me % 2 == 0
    pair = jnp.stack([jnp.where(low_first, part, partner), jnp.where(low_first, partner, part)])
    received = [pair] + [shifted(pair, "tp", 2 * k) for k in range(1, n_x)]
    stacked = jnp.stack(received)
    order = (mine_x - jnp.arange(n_x, dtype=jnp.int32)) % n_x
    full = jnp.take(stacked, order, axis=0)
    return full.transpose(2, 0, 1, 3).reshape(rows, n_x * 2 * width)


def tp_reduce(full):
    rows, total_width = full.shape
    n_x = lax.axis_size("tp") // 2
    me = lax.axis_index("tp")
    mine_x = me // 2
    pieces = full.reshape(rows, n_x, total_width // n_x)
    acc = jnp.take(pieces, mine_x, axis=1).astype(jnp.float32)
    for k in range(1, n_x):
        piece = jnp.take(pieces, (mine_x + k) % n_x, axis=1)
        acc = acc + shifted(piece, "tp", 2 * k).astype(jnp.float32)
    halves = acc.reshape(rows, 2, total_width // n_x // 2)
    low = me % 2 == 0
    mine = jnp.where(low, halves[:, 0], halves[:, 1])
    other = jnp.where(low, halves[:, 1], halves[:, 0])
    got = swapped(other.astype(jnp.bfloat16), "tp", 0)
    return mine + got.astype(jnp.float32)


def rms_normed(values, gain):
    square = jnp.mean(values * values, axis=-1, keepdims=True)
    return (values * lax.rsqrt(square + EPSILON) * gain).astype(jnp.bfloat16)


def rotate(vectors, positions):
    half = vectors.shape[-1] // 2
    exponent = jnp.arange(half, dtype=jnp.float32) * (-2.0 / vectors.shape[-1])
    freqs = jnp.power(jnp.float32(10000.0), exponent)
    angles = positions.astype(jnp.float32)[:, None] * freqs[None, :]
    cosine = jnp.cos(angles)[:, None, :]
    sine = jnp.sin(angles)[:, None, :]
    first = vectors[..., :half]
    second = vectors[..., half:]
    return jnp.concatenate(
        [first * cosine - second * sine, second * cosine + first * sine], axis=-1
    )


def partial_attention(query, keys, values, valid):
    scores = jnp.einsum("pbcgd,pkcd->pbcgk", query, keys, preferred_element_type=jnp.float32) * 0.125
    scores = jnp.where(valid, scores, SENTINEL)
    top = jnp.max(scores, axis=-1)
    weights = jnp.where(valid, jnp.exp(scores - top[..., None]), 0.0)
    total = jnp.sum(weights, axis=-1)
    weighted = jnp.einsum(
        "pbcgk,pkcd->pbcgd", weights.astype(jnp.bfloat16), values, preferred_element_type=jnp.float32
    )
    return (weighted, top, total)


def on_device(
    tok_ids,
    accept,
    sub_ids,
    cache_len,
    spill,
    embed,
    attn_gain,
    w_query,
    w_key,
    w_value,
    w_out,
    mlp_gain,
    w_gate,
    w_up,
    w_down,
    cache_keys,
    cache_values,
):
    block = tok_ids.shape[0]
    slots = cache_keys.shape[0]
    query_local = w_query.shape[1] // HD
    stored_local = w_key.shape[1] // HD
    per_stored = query_local // stored_local
    group_index = lax.axis_index("grp")
    own_count = cache_len[group_index] - spill[group_index]
    far_count = spill[group_index]
    positions = cache_len[group_index] + jnp.arange(block, dtype=jnp.int32)
    slot_ids = jnp.arange(slots, dtype=jnp.int32)
    tail_ids = slot_ids[block:]
    store_keys = cache_keys.reshape(slots, stored_local, HD)
    store_values = cache_values.reshape(slots, stored_local, HD)
    second_ids = jnp.where(accept == 1, sub_ids, tok_ids)

    table = lax.all_gather(embed, "grp", axis=0, tiled=True)
    both_ids = jnp.concatenate([tok_ids, second_ids])
    x_part = jnp.take(table, both_ids, axis=0)
    rows, width = x_part.shape

    tail_keys, tail_values = swapped((cache_keys[block:], cache_values[block:]), "grp", 0)
    far_keys = tail_keys.reshape(slots - block, stored_local, HD)
    far_values = tail_values.reshape(slots - block, stored_local, HD)
    far_valid = tail_ids >= slots - far_count
    own_valid = slot_ids < own_count
    valid = jnp.concatenate([own_valid, far_valid, jnp.ones((block,), dtype=bool)])

    x_full = tp_gather(x_part)
    normed = rms_normed(x_full.astype(jnp.float32), attn_gain)
    both_positions = jnp.concatenate([positions, positions])
    query = rotate(
        jnp.dot(normed, w_query, preferred_element_type=jnp.float32).reshape(
            rows, query_local, HD
        ),
        both_positions,
    )
    query = query.astype(jnp.bfloat16).reshape(2, block, stored_local, per_stored, HD)
    new_keys = rotate(
        jnp.dot(normed, w_key, preferred_element_type=jnp.float32).reshape(
            rows, stored_local, HD
        ),
        both_positions,
    ).astype(jnp.bfloat16).reshape(2, block, stored_local, HD)
    new_values = (
        jnp.dot(normed, w_value, preferred_element_type=jnp.float32)
        .reshape(2, block, stored_local, HD)
        .astype(jnp.bfloat16)
    )
    cached_keys = jnp.concatenate([store_keys, far_keys], axis=0)
    cached_values = jnp.concatenate([store_values, far_values], axis=0)
    keys = jnp.concatenate(
        [jnp.broadcast_to(cached_keys[None], (2,) + cached_keys.shape), new_keys], axis=1
    )
    values = jnp.concatenate(
        [jnp.broadcast_to(cached_values[None], (2,) + cached_values.shape), new_values], axis=1
    )
    weighted, top, total = partial_attention(query, keys, values, valid)
    attended = weighted / total[..., None]
    mixed = attended.reshape(rows, query_local * HD).astype(jnp.bfloat16)
    head_term = jnp.dot(mixed, w_out, preferred_element_type=jnp.float32)
    head_sum = tp_reduce(head_term.astype(jnp.bfloat16))
    resid_part = (x_part.astype(jnp.float32) + head_sum).astype(jnp.bfloat16)
    resid_full = tp_gather(resid_part)
    normed_mlp = rms_normed(resid_full.astype(jnp.float32), mlp_gain)
    gate = jnp.dot(normed_mlp, w_gate, preferred_element_type=jnp.float32)
    lift = jnp.dot(normed_mlp, w_up, preferred_element_type=jnp.float32)
    hidden = (jax.nn.silu(gate) * lift).astype(jnp.bfloat16)
    down_term = jnp.dot(hidden, w_down, preferred_element_type=jnp.float32)
    down_part = tp_reduce(down_term.astype(jnp.bfloat16))
    out = (resid_part.astype(jnp.float32) + down_part).astype(jnp.bfloat16)
    return (out[:block], out[block:])


def solution(mesh):
    placed = (
        P("grp"),
        P("grp"),
        P("grp"),
        P(),
        P(),
        P("grp", "tp"),
        P(),
        P(None, "tp"),
        P(None, "tp"),
        P(None, "tp"),
        P("tp", None),
        P(),
        P(None, "tp"),
        P(None, "tp"),
        P("tp", None),
        P("grp", "tp"),
        P("grp", "tp"),
    )
    return jax.shard_map(
        on_device,
        mesh=mesh,
        in_specs=placed,
        out_specs=(P("grp", "tp"), P("grp", "tp")),
        check_vma=False,
    )
```

```python
import jax
import jax.numpy as jnp
from jax import lax
from jax.sharding import PartitionSpec as P
from jax.experimental import pallas as pl
from jax.experimental.pallas import tpu as pltpu

HD = 64


EPSILON = 1e-05
SENTINEL = -1e30


def shifted(array, axis, step):
    n = lax.axis_size(axis)
    return lax.ppermute(array, axis, [(i, (i + step) % n) for i in range(n)])


def swapped(array, axis, bit):
    return lax.ppermute(array, axis, [(i, i ^ 1 << bit) for i in range(lax.axis_size(axis))])


def tp_gather(part):
    rows, width = part.shape
    n_x = lax.axis_size("tp") // 2
    me = lax.axis_index("tp")
    mine_x = me // 2
    partner = swapped(part, "tp", 0)
    low_first = me % 2 == 0
    pair = jnp.where(
        low_first,
        jnp.concatenate([part, partner], axis=1),
        jnp.concatenate([partner, part], axis=1),
    )
    full = jnp.zeros((rows, n_x * 2 * width), part.dtype)
    full = lax.dynamic_update_slice(full, pair, (0, mine_x * 2 * width))
    for k in range(1, n_x):
        got = shifted(pair, "tp", 2 * k)
        full = lax.dynamic_update_slice(full, got, (0, ((mine_x - k) % n_x) * 2 * width))
    return full


def tp_reduce(full):
    rows, total_width = full.shape
    n_x = lax.axis_size("tp") // 2
    me = lax.axis_index("tp")
    mine_x = me // 2
    span = total_width // n_x
    acc = lax.dynamic_slice_in_dim(full, mine_x * span, span, 1).astype(jnp.float32)
    for k in range(1, n_x):
        piece = lax.dynamic_slice_in_dim(full, ((mine_x + k) % n_x) * span, span, 1)
        acc = acc + shifted(piece, "tp", 2 * k).astype(jnp.float32)
    halves = acc.reshape(rows, 2, total_width // n_x // 2)
    low = me % 2 == 0
    mine = jnp.where(low, halves[:, 0], halves[:, 1])
    other = jnp.where(low, halves[:, 1], halves[:, 0])
    got = swapped(other.astype(jnp.bfloat16), "tp", 0)
    return mine + got.astype(jnp.float32)


def rms_normed(values, gain):
    square = jnp.mean(values * values, axis=-1, keepdims=True)
    return (values * lax.rsqrt(square + EPSILON) * gain).astype(jnp.bfloat16)


def rotate(vectors, positions):
    half = vectors.shape[-1] // 2
    exponent = jnp.arange(half, dtype=jnp.float32) * (-2.0 / vectors.shape[-1])
    freqs = jnp.power(jnp.float32(10000.0), exponent)
    angles = positions.astype(jnp.float32)[:, None] * freqs[None, :]
    cosine = jnp.cos(angles)[:, None, :]
    sine = jnp.sin(angles)[:, None, :]
    first = vectors[..., :half]
    second = vectors[..., half:]
    return jnp.concatenate(
        [first * cosine - second * sine, second * cosine + first * sine], axis=-1
    )


def attention_kernel(q_ref, ko_ref, kf_ref, kn_ref, vo_ref, vf_ref, vn_ref, mo_ref, mf_ref, o_ref):
    query = q_ref[0]
    contract = (((1,), (1,)), ((), ()))
    parts = []
    for keys, mask in ((ko_ref[...], mo_ref[...]), (kf_ref[...], mf_ref[...]), (kn_ref[0], None)):
        scores = lax.dot_general(query, keys, contract, preferred_element_type=jnp.float32) * 0.125
        if mask is not None:
            scores = jnp.where(mask > 0, scores, SENTINEL)
        parts.append((scores, mask))
    top = parts[0][0].max(axis=-1, keepdims=True)
    for scores, _ in parts[1:]:
        top = jnp.maximum(top, scores.max(axis=-1, keepdims=True))
    total = jnp.zeros_like(top)
    weighted = jnp.zeros((query.shape[0], vn_ref.shape[-1]), jnp.float32)
    for (scores, mask), values in zip(parts, (vo_ref[...], vf_ref[...], vn_ref[0])):
        weights = jnp.exp(scores - top)
        if mask is not None:
            weights = jnp.where(mask > 0, weights, 0.0)
        total = total + weights.sum(axis=-1, keepdims=True)
        weighted = weighted + jnp.dot(
            weights.astype(jnp.bfloat16), values, preferred_element_type=jnp.float32
        )
    o_ref[0] = (weighted / total).astype(o_ref.dtype)


def attention(query, own_keys, far_keys, new_keys, own_values, far_values, new_values, own_mask, far_mask):
    passes, rows, depth = query.shape
    tile = 256
    n_own = own_keys.shape[0]
    n_far = far_keys.shape[0]
    n_new = new_keys.shape[1]
    n_keys = n_own + n_far + n_new
    whole = lambda shape: pl.BlockSpec(shape, lambda p, i: (0,) * len(shape))
    per_pass = pl.BlockSpec((1, n_new, depth), lambda p, i: (p, 0, 0))
    return pl.pallas_call(
        attention_kernel,
        grid=(passes, rows // tile),
        in_specs=[
            pl.BlockSpec((1, tile, depth), lambda p, i: (p, i, 0)),
            whole((n_own, depth)),
            whole((n_far, depth)),
            per_pass,
            whole((n_own, depth)),
            whole((n_far, depth)),
            per_pass,
            whole((1, n_own)),
            whole((1, n_far)),
        ],
        out_specs=pl.BlockSpec((1, tile, depth), lambda p, i: (p, i, 0)),
        out_shape=jax.ShapeDtypeStruct(query.shape, jnp.bfloat16),
        cost_estimate=pl.CostEstimate(
            flops=4 * passes * rows * n_keys * depth,
            transcendentals=passes * rows * n_keys,
            bytes_accessed=2 * (2 * passes * rows * depth + 2 * n_keys * depth),
        ),
    )(query, own_keys, far_keys, new_keys, own_values, far_values, new_values, own_mask, far_mask)


def on_device(
    tok_ids,
    accept,
    sub_ids,
    cache_len,
    spill,
    embed,
    attn_gain,
    w_query,
    w_key,
    w_value,
    w_out,
    mlp_gain,
    w_gate,
    w_up,
    w_down,
    cache_keys,
    cache_values,
):
    block = tok_ids.shape[0]
    slots = cache_keys.shape[0]
    query_local = w_query.shape[1] // HD
    stored_local = w_key.shape[1] // HD
    per_stored = query_local // stored_local
    group_index = lax.axis_index("grp")
    own_count = cache_len[group_index] - spill[group_index]
    far_count = spill[group_index]
    positions = cache_len[group_index] + jnp.arange(block, dtype=jnp.int32)
    slot_ids = jnp.arange(slots, dtype=jnp.int32)
    tail_ids = slot_ids[block:]
    store_keys = cache_keys.reshape(slots, stored_local, HD)
    store_values = cache_values.reshape(slots, stored_local, HD)
    second_ids = jnp.where(accept == 1, sub_ids, tok_ids)

    table = lax.all_gather(embed, "grp", axis=0, tiled=True)
    both_ids = jnp.concatenate([tok_ids, second_ids])
    x_part = jnp.take(table, both_ids, axis=0)
    rows, width = x_part.shape

    tail_keys, tail_values = swapped((cache_keys[block:], cache_values[block:]), "grp", 0)
    far_keys = tail_keys.reshape(slots - block, stored_local, HD)
    far_values = tail_values.reshape(slots - block, stored_local, HD)
    far_valid = tail_ids >= slots - far_count
    own_valid = slot_ids < own_count

    x_full = tp_gather(x_part)
    normed = rms_normed(x_full.astype(jnp.float32), attn_gain)
    both_positions = jnp.concatenate([positions, positions])
    query = rotate(
        jnp.dot(normed, w_query, preferred_element_type=jnp.float32).reshape(
            rows, query_local, HD
        ),
        both_positions,
    )
    query = query.astype(jnp.bfloat16).reshape(2, block, stored_local, per_stored, HD)
    new_keys = rotate(
        jnp.dot(normed, w_key, preferred_element_type=jnp.float32).reshape(
            rows, stored_local, HD
        ),
        both_positions,
    ).astype(jnp.bfloat16).reshape(2, block, stored_local, HD)
    new_values = (
        jnp.dot(normed, w_value, preferred_element_type=jnp.float32)
        .reshape(2, block, stored_local, HD)
        .astype(jnp.bfloat16)
    )
    mixed_heads = attention(
        query.reshape(2, block * per_stored, HD),
        store_keys.reshape(slots, HD),
        far_keys.reshape(slots - block, HD),
        new_keys.reshape(2, block, HD),
        store_values.reshape(slots, HD),
        far_values.reshape(slots - block, HD),
        new_values.reshape(2, block, HD),
        own_valid.astype(jnp.int32)[None],
        far_valid.astype(jnp.int32)[None],
    )
    mixed = mixed_heads.reshape(rows, query_local * HD)
    head_term = jnp.dot(mixed, w_out, preferred_element_type=jnp.float32)
    head_sum = tp_reduce(head_term.astype(jnp.bfloat16))
    resid_part = (x_part.astype(jnp.float32) + head_sum).astype(jnp.bfloat16)
    resid_full = tp_gather(resid_part)
    normed_mlp = rms_normed(resid_full.astype(jnp.float32), mlp_gain)
    gate = jnp.dot(normed_mlp, w_gate, preferred_element_type=jnp.float32)
    lift = jnp.dot(normed_mlp, w_up, preferred_element_type=jnp.float32)
    hidden = (jax.nn.silu(gate) * lift).astype(jnp.bfloat16)
    down_term = jnp.dot(hidden, w_down, preferred_element_type=jnp.float32)
    down_part = tp_reduce(down_term.astype(jnp.bfloat16))
    out = (resid_part.astype(jnp.float32) + down_part).astype(jnp.bfloat16)
    return (out[:block], out[block:])


def solution(mesh):
    placed = (
        P("grp"),
        P("grp"),
        P("grp"),
        P(),
        P(),
        P("grp", "tp"),
        P(),
        P(None, "tp"),
        P(None, "tp"),
        P(None, "tp"),
        P("tp", None),
        P(),
        P(None, "tp"),
        P(None, "tp"),
        P("tp", None),
        P("grp", "tp"),
        P("grp", "tp"),
    )
    return jax.shard_map(
        on_device,
        mesh=mesh,
        in_specs=placed,
        out_specs=(P("grp", "tp"), P("grp", "tp")),
        check_vma=False,
    )
```

```python
import jax
import jax.numpy as jnp
from jax import lax
from jax.sharding import Mesh, PartitionSpec as P
from jax.experimental import pallas as pl
from jax.experimental.pallas import tpu as pltpu

HD = 64
GRP = ("chips", "core")


EPSILON = 1e-05
SENTINEL = -1e30


def shifted(array, axis, step):
    n = lax.axis_size(axis)
    return lax.ppermute(array, axis, [(i, (i + step) % n) for i in range(n)])


def swapped(array, axis, bit):
    return lax.ppermute(array, axis, [(i, i ^ 1 << bit) for i in range(lax.axis_size(axis))])


def x_gather(pair):
    rows, span = pair.shape
    n_x = lax.axis_size("tp") // 2
    mine_x = lax.axis_index("tp") // 2
    full = jnp.zeros((rows, n_x * span), pair.dtype)
    full = lax.dynamic_update_slice(full, pair, (0, mine_x * span))
    for k in range(1, n_x):
        got = shifted(pair, "tp", 2 * k)
        full = lax.dynamic_update_slice(full, got, (0, ((mine_x - k) % n_x) * span))
    return full


def tp_gather(part):
    me = lax.axis_index("tp")
    partner = swapped(part, "tp", 0)
    pair = jnp.where(
        me % 2 == 0,
        jnp.concatenate([part, partner], axis=1),
        jnp.concatenate([partner, part], axis=1),
    )
    return x_gather(pair)


def x_reduce(full):
    rows, total_width = full.shape
    n_x = lax.axis_size("tp") // 2
    mine_x = lax.axis_index("tp") // 2
    span = total_width // n_x
    acc = lax.dynamic_slice_in_dim(full, mine_x * span, span, 1).astype(jnp.float32)
    for k in range(1, n_x):
        piece = lax.dynamic_slice_in_dim(full, ((mine_x + k) % n_x) * span, span, 1)
        acc = acc + shifted(piece, "tp", 2 * k).astype(jnp.float32)
    return acc


def tp_reduce(full):
    me = lax.axis_index("tp")
    acc = x_reduce(full)
    rows, span = acc.shape
    halves = acc.reshape(rows, 2, span // 2)
    low = me % 2 == 0
    mine = jnp.where(low, halves[:, 0], halves[:, 1])
    other = jnp.where(low, halves[:, 1], halves[:, 0])
    got = swapped(other.astype(jnp.bfloat16), "tp", 0)
    return mine + got.astype(jnp.float32)


def pair_reduce(full):
    rounded = x_reduce(full).astype(jnp.bfloat16)
    return rounded.astype(jnp.float32) + swapped(rounded, "tp", 0).astype(jnp.float32)


def rms_normed(values, gain):
    square = jnp.mean(values * values, axis=-1, keepdims=True)
    return (values * lax.rsqrt(square + EPSILON) * gain).astype(jnp.bfloat16)


def rotate(vectors, positions):
    half = vectors.shape[-1] // 2
    exponent = jnp.arange(half, dtype=jnp.float32) * (-2.0 / vectors.shape[-1])
    freqs = jnp.power(jnp.float32(10000.0), exponent)
    angles = positions.astype(jnp.float32)[:, None] * freqs[None, :]
    cosine = jnp.cos(angles)[:, None, :]
    sine = jnp.sin(angles)[:, None, :]
    first = vectors[..., :half]
    second = vectors[..., half:]
    return jnp.concatenate(
        [first * cosine - second * sine, second * cosine + first * sine], axis=-1
    )


def attention_kernel(q_ref, ko_ref, kf_ref, kn_ref, vo_ref, vf_ref, vn_ref, mo_ref, mf_ref, o_ref):
    query = q_ref[0]
    contract = (((1,), (1,)), ((), ()))
    parts = []
    for keys, mask in ((ko_ref[...], mo_ref[...]), (kf_ref[...], mf_ref[...]), (kn_ref[0], None)):
        scores = lax.dot_general(query, keys, contract, preferred_element_type=jnp.float32) * 0.125
        if mask is not None:
            scores = jnp.where(mask > 0, scores, SENTINEL)
        parts.append((scores, mask))
    top = parts[0][0].max(axis=-1, keepdims=True)
    for scores, _ in parts[1:]:
        top = jnp.maximum(top, scores.max(axis=-1, keepdims=True))
    total = jnp.zeros_like(top)
    weighted = jnp.zeros((query.shape[0], vn_ref.shape[-1]), jnp.float32)
    for (scores, mask), values in zip(parts, (vo_ref[...], vf_ref[...], vn_ref[0])):
        weights = jnp.exp(scores - top)
        if mask is not None:
            weights = jnp.where(mask > 0, weights, 0.0)
        total = total + weights.sum(axis=-1, keepdims=True)
        weighted = weighted + jnp.dot(
            weights.astype(jnp.bfloat16), values, preferred_element_type=jnp.float32
        )
    o_ref[0] = (weighted / total).astype(o_ref.dtype)


def attention(query, own_keys, far_keys, new_keys, own_values, far_values, new_values, own_mask, far_mask):
    passes, rows, depth = query.shape
    tile = 256
    n_own = own_keys.shape[0]
    n_far = far_keys.shape[0]
    n_new = new_keys.shape[1]
    n_keys = n_own + n_far + n_new
    whole = lambda shape: pl.BlockSpec(shape, lambda p, i: (0,) * len(shape))
    per_pass = pl.BlockSpec((1, n_new, depth), lambda p, i: (p, 0, 0))
    return pl.pallas_call(
        attention_kernel,
        grid=(passes, rows // tile),
        in_specs=[
            pl.BlockSpec((1, tile, depth), lambda p, i: (p, i, 0)),
            whole((n_own, depth)),
            whole((n_far, depth)),
            per_pass,
            whole((n_own, depth)),
            whole((n_far, depth)),
            per_pass,
            whole((1, n_own)),
            whole((1, n_far)),
        ],
        out_specs=pl.BlockSpec((1, tile, depth), lambda p, i: (p, i, 0)),
        out_shape=jax.ShapeDtypeStruct(query.shape, jnp.bfloat16),
        cost_estimate=pl.CostEstimate(
            flops=4 * passes * rows * n_keys * depth,
            transcendentals=passes * rows * n_keys,
            bytes_accessed=2 * (2 * passes * rows * depth + 2 * n_keys * depth),
        ),
    )(query, own_keys, far_keys, new_keys, own_values, far_values, new_values, own_mask, far_mask)


def on_device(
    tok_ids,
    accept,
    sub_ids,
    cache_len,
    spill,
    embed,
    attn_gain,
    w_query,
    w_key,
    w_value,
    w_out,
    mlp_gain,
    w_gate,
    w_up,
    w_down,
    cache_keys,
    cache_values,
):
    block = tok_ids.shape[0]
    slots = cache_keys.shape[0]
    query_local = w_query.shape[1] // HD
    stored_local = w_key.shape[1] // HD
    per_stored = query_local // stored_local
    group_index = lax.axis_index(GRP)
    own_count = cache_len[group_index] - spill[group_index]
    far_count = spill[group_index]
    positions = cache_len[group_index] + jnp.arange(block, dtype=jnp.int32)
    slot_ids = jnp.arange(slots, dtype=jnp.int32)
    tail_ids = slot_ids[block:]
    store_keys = cache_keys.reshape(slots, stored_local, HD)
    store_values = cache_values.reshape(slots, stored_local, HD)
    second_ids = jnp.where(accept == 1, sub_ids, tok_ids)

    local_vocab = embed.shape[0]
    core = lax.axis_index("core")
    half = lax.all_gather(embed, "chips", axis=0, tiled=True)
    other_half = lax.ppermute(half, "core", [(0, 1), (1, 0)])
    both_ids = jnp.concatenate([tok_ids, second_ids])
    owner = both_ids // local_vocab
    at = (owner // 2) * local_vocab + both_ids % local_vocab
    x_part = jnp.where(
        (owner % 2 == core)[:, None],
        jnp.take(half, at, axis=0),
        jnp.take(other_half, at, axis=0),
    )
    rows, width = x_part.shape

    tail_keys, tail_values = lax.ppermute(
        (cache_keys[block:], cache_values[block:]), "core", [(0, 1), (1, 0)]
    )
    far_keys = tail_keys.reshape(slots - block, stored_local, HD)
    far_values = tail_values.reshape(slots - block, stored_local, HD)
    far_valid = tail_ids >= slots - far_count
    own_valid = slot_ids < own_count

    x_full = tp_gather(x_part)
    normed = rms_normed(x_full.astype(jnp.float32), attn_gain)
    both_positions = jnp.concatenate([positions, positions])
    query = rotate(
        jnp.dot(normed, w_query, preferred_element_type=jnp.float32).reshape(
            rows, query_local, HD
        ),
        both_positions,
    )
    query = query.astype(jnp.bfloat16).reshape(2, block, stored_local, per_stored, HD)
    new_keys = rotate(
        jnp.dot(normed, w_key, preferred_element_type=jnp.float32).reshape(
            rows, stored_local, HD
        ),
        both_positions,
    ).astype(jnp.bfloat16).reshape(2, block, stored_local, HD)
    new_values = (
        jnp.dot(normed, w_value, preferred_element_type=jnp.float32)
        .reshape(2, block, stored_local, HD)
        .astype(jnp.bfloat16)
    )
    mixed_heads = attention(
        query.reshape(2, block * per_stored, HD),
        store_keys.reshape(slots, HD),
        far_keys.reshape(slots - block, HD),
        new_keys.reshape(2, block, HD),
        store_values.reshape(slots, HD),
        far_values.reshape(slots - block, HD),
        new_values.reshape(2, block, HD),
        own_valid.astype(jnp.int32)[None],
        far_valid.astype(jnp.int32)[None],
    )
    mixed = mixed_heads.reshape(rows, query_local * HD)
    head_term = jnp.dot(mixed, w_out, preferred_element_type=jnp.float32)
    head_pair = pair_reduce(head_term.astype(jnp.bfloat16))
    span = head_pair.shape[1]
    mine_x = lax.axis_index("tp") // 2
    x_pair = lax.dynamic_slice_in_dim(x_full, mine_x * span, span, 1)
    resid_pair = (x_pair.astype(jnp.float32) + head_pair).astype(jnp.bfloat16)
    resid_full = x_gather(resid_pair)
    resid_part = lax.dynamic_slice_in_dim(resid_pair, (lax.axis_index("tp") % 2) * width, width, 1)
    normed_mlp = rms_normed(resid_full.astype(jnp.float32), mlp_gain)
    gate = jnp.dot(normed_mlp, w_gate, preferred_element_type=jnp.float32)
    lift = jnp.dot(normed_mlp, w_up, preferred_element_type=jnp.float32)
    hidden = (jax.nn.silu(gate) * lift).astype(jnp.bfloat16)
    down_term = jnp.dot(hidden, w_down, preferred_element_type=jnp.float32)
    down_part = tp_reduce(down_term.astype(jnp.bfloat16))
    out = (resid_part.astype(jnp.float32) + down_part).astype(jnp.bfloat16)
    return (out[:block], out[block:])


def solution(mesh):
    n_grp, n_tp = mesh.shape["grp"], mesh.shape["tp"]
    mesh = Mesh(mesh.devices.reshape(n_grp // 2, 2, n_tp), ("chips", "core", "tp"))
    placed = (
        P(GRP),
        P(GRP),
        P(GRP),
        P(),
        P(),
        P(GRP, "tp"),
        P(),
        P(None, "tp"),
        P(None, "tp"),
        P(None, "tp"),
        P("tp", None),
        P(),
        P(None, "tp"),
        P(None, "tp"),
        P("tp", None),
        P(GRP, "tp"),
        P(GRP, "tp"),
    )
    return jax.shard_map(
        on_device,
        mesh=mesh,
        in_specs=placed,
        out_specs=(P(GRP, "tp"), P(GRP, "tp")),
        check_vma=False,
    )
```

```python
import jax
import jax.numpy as jnp
from jax import lax
from jax.sharding import PartitionSpec as P
from jax.experimental import pallas as pl
from jax.experimental.pallas import tpu as pltpu

HD = 64
GRP = "grp"


EPSILON = 1e-05
SENTINEL = -1e30


def shifted(array, axis, step):
    n = lax.axis_size(axis)
    return lax.ppermute(array, axis, [(i, (i + step) % n) for i in range(n)])


def swapped(array, axis, bit):
    return lax.ppermute(array, axis, [(i, i ^ 1 << bit) for i in range(lax.axis_size(axis))])


def x_gather(pair):
    rows, span = pair.shape
    n_x = lax.axis_size("tp") // 2
    mine_x = lax.axis_index("tp") // 2
    full = jnp.zeros((rows, n_x * span), pair.dtype)
    full = lax.dynamic_update_slice(full, pair, (0, mine_x * span))
    for k in range(1, n_x):
        got = shifted(pair, "tp", 2 * k)
        full = lax.dynamic_update_slice(full, got, (0, ((mine_x - k) % n_x) * span))
    return full


def tp_gather(part):
    me = lax.axis_index("tp")
    partner = swapped(part, "tp", 0)
    pair = jnp.where(
        me % 2 == 0,
        jnp.concatenate([part, partner], axis=1),
        jnp.concatenate([partner, part], axis=1),
    )
    return x_gather(pair)


def x_reduce(full):
    rows, total_width = full.shape
    n_x = lax.axis_size("tp") // 2
    mine_x = lax.axis_index("tp") // 2
    span = total_width // n_x
    acc = lax.dynamic_slice_in_dim(full, mine_x * span, span, 1).astype(jnp.float32)
    for k in range(1, n_x):
        piece = lax.dynamic_slice_in_dim(full, ((mine_x + k) % n_x) * span, span, 1)
        acc = acc + shifted(piece, "tp", 2 * k).astype(jnp.float32)
    return acc


def tp_reduce(full):
    me = lax.axis_index("tp")
    acc = x_reduce(full)
    rows, span = acc.shape
    halves = acc.reshape(rows, 2, span // 2)
    low = me % 2 == 0
    mine = jnp.where(low, halves[:, 0], halves[:, 1])
    other = jnp.where(low, halves[:, 1], halves[:, 0])
    got = swapped(other.astype(jnp.bfloat16), "tp", 0)
    return mine + got.astype(jnp.float32)


def pair_reduce(full):
    rounded = x_reduce(full).astype(jnp.bfloat16)
    return rounded.astype(jnp.float32) + swapped(rounded, "tp", 0).astype(jnp.float32)


def rms_normed(values, gain):
    square = jnp.mean(values * values, axis=-1, keepdims=True)
    return (values * lax.rsqrt(square + EPSILON) * gain).astype(jnp.bfloat16)


def rotate(vectors, positions):
    half = vectors.shape[-1] // 2
    exponent = jnp.arange(half, dtype=jnp.float32) * (-2.0 / vectors.shape[-1])
    freqs = jnp.power(jnp.float32(10000.0), exponent)
    angles = positions.astype(jnp.float32)[:, None] * freqs[None, :]
    cosine = jnp.cos(angles)[:, None, :]
    sine = jnp.sin(angles)[:, None, :]
    first = vectors[..., :half]
    second = vectors[..., half:]
    return jnp.concatenate(
        [first * cosine - second * sine, second * cosine + first * sine], axis=-1
    )


def attention_kernel(q_ref, ko_ref, kf_ref, kn_ref, vo_ref, vf_ref, vn_ref, mo_ref, mf_ref, o_ref):
    query = q_ref[0]
    contract = (((1,), (1,)), ((), ()))
    parts = []
    for keys, mask in ((ko_ref[...], mo_ref[...]), (kf_ref[...], mf_ref[...]), (kn_ref[0], None)):
        scores = lax.dot_general(query, keys, contract, preferred_element_type=jnp.float32) * 0.125
        if mask is not None:
            scores = jnp.where(mask > 0, scores, SENTINEL)
        parts.append((scores, mask))
    top = parts[0][0].max(axis=-1, keepdims=True)
    for scores, _ in parts[1:]:
        top = jnp.maximum(top, scores.max(axis=-1, keepdims=True))
    total = jnp.zeros_like(top)
    weighted = jnp.zeros((query.shape[0], vn_ref.shape[-1]), jnp.float32)
    for (scores, mask), values in zip(parts, (vo_ref[...], vf_ref[...], vn_ref[0])):
        weights = jnp.exp(scores - top)
        if mask is not None:
            weights = jnp.where(mask > 0, weights, 0.0)
        total = total + weights.sum(axis=-1, keepdims=True)
        weighted = weighted + jnp.dot(
            weights.astype(jnp.bfloat16), values, preferred_element_type=jnp.float32
        )
    o_ref[0] = (weighted / total).astype(o_ref.dtype)


def attention(query, own_keys, far_keys, new_keys, own_values, far_values, new_values, own_mask, far_mask):
    passes, rows, depth = query.shape
    tile = 256
    n_own = own_keys.shape[0]
    n_far = far_keys.shape[0]
    n_new = new_keys.shape[1]
    n_keys = n_own + n_far + n_new
    whole = lambda shape: pl.BlockSpec(shape, lambda p, i: (0,) * len(shape))
    per_pass = pl.BlockSpec((1, n_new, depth), lambda p, i: (p, 0, 0))
    return pl.pallas_call(
        attention_kernel,
        grid=(passes, rows // tile),
        in_specs=[
            pl.BlockSpec((1, tile, depth), lambda p, i: (p, i, 0)),
            whole((n_own, depth)),
            whole((n_far, depth)),
            per_pass,
            whole((n_own, depth)),
            whole((n_far, depth)),
            per_pass,
            whole((1, n_own)),
            whole((1, n_far)),
        ],
        out_specs=pl.BlockSpec((1, tile, depth), lambda p, i: (p, i, 0)),
        out_shape=jax.ShapeDtypeStruct(query.shape, jnp.bfloat16),
        cost_estimate=pl.CostEstimate(
            flops=4 * passes * rows * n_keys * depth,
            transcendentals=passes * rows * n_keys,
            bytes_accessed=2 * (2 * passes * rows * depth + 2 * n_keys * depth),
        ),
    )(query, own_keys, far_keys, new_keys, own_values, far_values, new_values, own_mask, far_mask)


def on_device(
    tok_ids,
    accept,
    sub_ids,
    cache_len,
    spill,
    embed,
    attn_gain,
    w_query,
    w_key,
    w_value,
    w_out,
    mlp_gain,
    w_gate,
    w_up,
    w_down,
    cache_keys,
    cache_values,
):
    block = tok_ids.shape[0]
    slots = cache_keys.shape[0]
    query_local = w_query.shape[1] // HD
    stored_local = w_key.shape[1] // HD
    per_stored = query_local // stored_local
    group_index = lax.axis_index(GRP)
    own_count = cache_len[group_index] - spill[group_index]
    far_count = spill[group_index]
    positions = cache_len[group_index] + jnp.arange(block, dtype=jnp.int32)
    slot_ids = jnp.arange(slots, dtype=jnp.int32)
    tail_ids = slot_ids[block:]
    store_keys = cache_keys.reshape(slots, stored_local, HD)
    store_values = cache_values.reshape(slots, stored_local, HD)
    second_ids = jnp.where(accept == 1, sub_ids, tok_ids)

    table = lax.all_gather(embed, GRP, axis=0, tiled=True)
    both_ids = jnp.concatenate([tok_ids, second_ids])
    x_part = jnp.take(table, both_ids, axis=0)
    rows, width = x_part.shape

    tail_keys, tail_values = swapped((cache_keys[block:], cache_values[block:]), GRP, 0)
    far_keys = tail_keys.reshape(slots - block, stored_local, HD)
    far_values = tail_values.reshape(slots - block, stored_local, HD)
    far_valid = tail_ids >= slots - far_count
    own_valid = slot_ids < own_count

    own_mask = own_valid.astype(jnp.int32)[None]
    far_mask = far_valid.astype(jnp.int32)[None]
    mine_x = lax.axis_index("tp") // 2

    def after(value, stage, lead):
        if lead is None:
            return value
        return lax.optimization_barrier((value, lead[stage]))[0]

    def denoise(x_part, lead=None):
        marks = {}
        x_full = tp_gather(x_part)
        marks["gathered"] = x_full
        x_full = after(x_full, "attended", lead)
        normed = rms_normed(x_full.astype(jnp.float32), attn_gain)
        query = rotate(
            jnp.dot(normed, w_query, preferred_element_type=jnp.float32).reshape(
                block, query_local, HD
            ),
            positions,
        ).astype(jnp.bfloat16)
        new_keys = rotate(
            jnp.dot(normed, w_key, preferred_element_type=jnp.float32).reshape(
                block, stored_local, HD
            ),
            positions,
        ).astype(jnp.bfloat16)
        new_values = jnp.dot(normed, w_value, preferred_element_type=jnp.float32).astype(
            jnp.bfloat16
        )
        mixed_heads = attention(
            query.reshape(1, block * per_stored, HD),
            store_keys.reshape(slots, HD),
            far_keys.reshape(slots - block, HD),
            new_keys.reshape(1, block, HD),
            store_values.reshape(slots, HD),
            far_values.reshape(slots - block, HD),
            new_values.reshape(1, block, HD),
            own_mask,
            far_mask,
        )
        mixed = mixed_heads.reshape(block, query_local * HD)
        head_term = jnp.dot(mixed, w_out, preferred_element_type=jnp.float32)
        marks["attended"] = head_term
        head_pair = pair_reduce(head_term.astype(jnp.bfloat16))
        span = head_pair.shape[1]
        x_pair = lax.dynamic_slice_in_dim(x_full, mine_x * span, span, 1)
        resid_pair = (x_pair.astype(jnp.float32) + head_pair).astype(jnp.bfloat16)
        resid_full = x_gather(resid_pair)
        resid_part = lax.dynamic_slice_in_dim(
            resid_pair, (lax.axis_index("tp") % 2) * width, width, 1
        )
        resid_full = after(resid_full, "lifted", lead)
        normed_mlp = rms_normed(resid_full.astype(jnp.float32), mlp_gain)
        gate = jnp.dot(normed_mlp, w_gate, preferred_element_type=jnp.float32)
        lift = jnp.dot(normed_mlp, w_up, preferred_element_type=jnp.float32)
        hidden = (jax.nn.silu(gate) * lift).astype(jnp.bfloat16)
        down_term = jnp.dot(hidden, w_down, preferred_element_type=jnp.float32)
        marks["lifted"] = down_term
        down_part = tp_reduce(down_term.astype(jnp.bfloat16))
        return (resid_part.astype(jnp.float32) + down_part).astype(jnp.bfloat16), marks

    first_out, first_marks = denoise(x_part[:block])
    second_in = after(x_part[block:], "gathered", first_marks)
    second_out, _ = denoise(second_in, first_marks)
    return (first_out, second_out)


def solution(mesh):
    placed = (
        P(GRP),
        P(GRP),
        P(GRP),
        P(),
        P(),
        P(GRP, "tp"),
        P(),
        P(None, "tp"),
        P(None, "tp"),
        P(None, "tp"),
        P("tp", None),
        P(),
        P(None, "tp"),
        P(None, "tp"),
        P("tp", None),
        P(GRP, "tp"),
        P(GRP, "tp"),
    )
    return jax.shard_map(
        on_device,
        mesh=mesh,
        in_specs=placed,
        out_specs=(P(GRP, "tp"), P(GRP, "tp")),
        check_vma=False,
    )
```

```python
import jax
import jax.numpy as jnp
from jax import lax
from jax.sharding import PartitionSpec as P
from jax.experimental import pallas as pl
from jax.experimental.pallas import tpu as pltpu

HD = 64
GRP = "grp"


EPSILON = 1e-05
SENTINEL = -1e30


def shifted(array, axis, step):
    n = lax.axis_size(axis)
    return lax.ppermute(array, axis, [(i, (i + step) % n) for i in range(n)])


def swapped(array, axis, bit):
    return lax.ppermute(array, axis, [(i, i ^ 1 << bit) for i in range(lax.axis_size(axis))])


def rolled(array, axis, shift):
    n = array.shape[axis]
    doubled = jnp.concatenate([array, array], axis=axis)
    return lax.dynamic_slice_in_dim(doubled, shift, n, axis)


def x_gather(pair):
    n_x = lax.axis_size("tp") // 2
    got = [pair] + [shifted(pair, "tp", 2 * k) for k in range(1, n_x)]
    return jnp.concatenate([got[-j % n_x] for j in range(n_x)], axis=1)


def tp_gather(part):
    me = lax.axis_index("tp")
    partner = swapped(part, "tp", 0)
    pair = jnp.where(
        me % 2 == 0,
        jnp.concatenate([part, partner], axis=1),
        jnp.concatenate([partner, part], axis=1),
    )
    return x_gather(pair)


def x_reduce(full):
    rows, total_width = full.shape
    n_x = lax.axis_size("tp") // 2
    span = total_width // n_x
    acc = full[:, :span].astype(jnp.float32)
    for k in range(1, n_x):
        piece = full[:, k * span : (k + 1) * span]
        acc = acc + shifted(piece, "tp", 2 * k).astype(jnp.float32)
    return acc


def tp_reduce(full):
    me = lax.axis_index("tp")
    acc = x_reduce(full)
    rows, span = acc.shape
    halves = acc.reshape(rows, 2, span // 2)
    low = me % 2 == 0
    mine = jnp.where(low, halves[:, 0], halves[:, 1])
    other = jnp.where(low, halves[:, 1], halves[:, 0])
    got = swapped(other.astype(jnp.bfloat16), "tp", 0)
    return mine + got.astype(jnp.float32)


def pair_reduce(full):
    rounded = x_reduce(full).astype(jnp.bfloat16)
    return rounded.astype(jnp.float32) + swapped(rounded, "tp", 0).astype(jnp.float32)


def rms_normed(values, gain):
    square = jnp.mean(values * values, axis=-1, keepdims=True)
    return (values * lax.rsqrt(square + EPSILON) * gain).astype(jnp.bfloat16)


def rotate(vectors, positions):
    half = vectors.shape[-1] // 2
    exponent = jnp.arange(half, dtype=jnp.float32) * (-2.0 / vectors.shape[-1])
    freqs = jnp.power(jnp.float32(10000.0), exponent)
    angles = positions.astype(jnp.float32)[:, None] * freqs[None, :]
    cosine = jnp.cos(angles)[:, None, :]
    sine = jnp.sin(angles)[:, None, :]
    first = vectors[..., :half]
    second = vectors[..., half:]
    return jnp.concatenate(
        [first * cosine - second * sine, second * cosine + first * sine], axis=-1
    )


def attention_kernel(q_ref, ko_ref, kf_ref, kn_ref, vo_ref, vf_ref, vn_ref, mo_ref, mf_ref, o_ref):
    query = q_ref[0]
    contract = (((1,), (1,)), ((), ()))
    parts = []
    for keys, mask in ((ko_ref[...], mo_ref[...]), (kf_ref[...], mf_ref[...]), (kn_ref[0], None)):
        scores = lax.dot_general(query, keys, contract, preferred_element_type=jnp.float32) * 0.125
        if mask is not None:
            scores = jnp.where(mask > 0, scores, SENTINEL)
        parts.append((scores, mask))
    top = parts[0][0].max(axis=-1, keepdims=True)
    for scores, _ in parts[1:]:
        top = jnp.maximum(top, scores.max(axis=-1, keepdims=True))
    total = jnp.zeros_like(top)
    weighted = jnp.zeros((query.shape[0], vn_ref.shape[-1]), jnp.float32)
    for (scores, mask), values in zip(parts, (vo_ref[...], vf_ref[...], vn_ref[0])):
        weights = jnp.exp(scores - top)
        if mask is not None:
            weights = jnp.where(mask > 0, weights, 0.0)
        total = total + weights.sum(axis=-1, keepdims=True)
        weighted = weighted + jnp.dot(
            weights.astype(jnp.bfloat16), values, preferred_element_type=jnp.float32
        )
    o_ref[0] = (weighted / total).astype(o_ref.dtype)


def attention(query, own_keys, far_keys, new_keys, own_values, far_values, new_values, own_mask, far_mask):
    passes, rows, depth = query.shape
    tile = 256
    n_own = own_keys.shape[0]
    n_far = far_keys.shape[0]
    n_new = new_keys.shape[1]
    n_keys = n_own + n_far + n_new
    whole = lambda shape: pl.BlockSpec(shape, lambda p, i: (0,) * len(shape))
    per_pass = pl.BlockSpec((1, n_new, depth), lambda p, i: (p, 0, 0))
    return pl.pallas_call(
        attention_kernel,
        grid=(passes, rows // tile),
        in_specs=[
            pl.BlockSpec((1, tile, depth), lambda p, i: (p, i, 0)),
            whole((n_own, depth)),
            whole((n_far, depth)),
            per_pass,
            whole((n_own, depth)),
            whole((n_far, depth)),
            per_pass,
            whole((1, n_own)),
            whole((1, n_far)),
        ],
        out_specs=pl.BlockSpec((1, tile, depth), lambda p, i: (p, i, 0)),
        out_shape=jax.ShapeDtypeStruct(query.shape, jnp.bfloat16),
        cost_estimate=pl.CostEstimate(
            flops=4 * passes * rows * n_keys * depth,
            transcendentals=passes * rows * n_keys,
            bytes_accessed=2 * (2 * passes * rows * depth + 2 * n_keys * depth),
        ),
    )(query, own_keys, far_keys, new_keys, own_values, far_values, new_values, own_mask, far_mask)


def on_device(
    tok_ids,
    accept,
    sub_ids,
    cache_len,
    spill,
    embed,
    attn_gain,
    w_query,
    w_key,
    w_value,
    w_out,
    mlp_gain,
    w_gate,
    w_up,
    w_down,
    cache_keys,
    cache_values,
):
    block = tok_ids.shape[0]
    slots = cache_keys.shape[0]
    query_local = w_query.shape[1] // HD
    stored_local = w_key.shape[1] // HD
    per_stored = query_local // stored_local
    group_index = lax.axis_index(GRP)
    own_count = cache_len[group_index] - spill[group_index]
    far_count = spill[group_index]
    positions = cache_len[group_index] + jnp.arange(block, dtype=jnp.int32)
    slot_ids = jnp.arange(slots, dtype=jnp.int32)
    tail_ids = slot_ids[block:]
    store_keys = cache_keys.reshape(slots, stored_local, HD)
    store_values = cache_values.reshape(slots, stored_local, HD)
    second_ids = jnp.where(accept == 1, sub_ids, tok_ids)

    table = lax.all_gather(embed, GRP, axis=0, tiled=True)
    both_ids = jnp.concatenate([tok_ids, second_ids])
    x_part = jnp.take(table, both_ids, axis=0)
    rows, width = x_part.shape

    tail_keys, tail_values = swapped((cache_keys[block:], cache_values[block:]), GRP, 0)
    far_keys = tail_keys.reshape(slots - block, stored_local, HD)
    far_values = tail_values.reshape(slots - block, stored_local, HD)
    far_valid = tail_ids >= slots - far_count
    own_valid = slot_ids < own_count

    own_mask = own_valid.astype(jnp.int32)[None]
    far_mask = far_valid.astype(jnp.int32)[None]
    mine_x = lax.axis_index("tp") // 2
    shift = mine_x * 2 * width
    attn_gain = rolled(attn_gain, 0, shift)
    mlp_gain = rolled(mlp_gain, 0, shift)
    w_query = rolled(w_query, 0, shift)
    w_key = rolled(w_key, 0, shift)
    w_value = rolled(w_value, 0, shift)
    w_gate = rolled(w_gate, 0, shift)
    w_up = rolled(w_up, 0, shift)
    w_out = rolled(w_out, 1, shift)
    w_down = rolled(w_down, 1, shift)

    def after(value, stage, lead):
        if lead is None:
            return value
        return lax.optimization_barrier((value, lead[stage]))[0]

    def denoise(x_part, lead=None):
        marks = {}
        x_full = tp_gather(x_part)
        marks["gathered"] = x_full
        x_full = after(x_full, "attended", lead)
        normed = rms_normed(x_full.astype(jnp.float32), attn_gain)
        query = rotate(
            jnp.dot(normed, w_query, preferred_element_type=jnp.float32).reshape(
                block, query_local, HD
            ),
            positions,
        ).astype(jnp.bfloat16)
        new_keys = rotate(
            jnp.dot(normed, w_key, preferred_element_type=jnp.float32).reshape(
                block, stored_local, HD
            ),
            positions,
        ).astype(jnp.bfloat16)
        new_values = jnp.dot(normed, w_value, preferred_element_type=jnp.float32).astype(
            jnp.bfloat16
        )
        mixed_heads = attention(
            query.reshape(1, block * per_stored, HD),
            store_keys.reshape(slots, HD),
            far_keys.reshape(slots - block, HD),
            new_keys.reshape(1, block, HD),
            store_values.reshape(slots, HD),
            far_values.reshape(slots - block, HD),
            new_values.reshape(1, block, HD),
            own_mask,
            far_mask,
        )
        mixed = mixed_heads.reshape(block, query_local * HD)
        head_term = jnp.dot(mixed, w_out, preferred_element_type=jnp.float32)
        marks["attended"] = head_term
        head_pair = pair_reduce(head_term.astype(jnp.bfloat16))
        span = head_pair.shape[1]
        x_pair = x_full[:, :span]
        resid_pair = (x_pair.astype(jnp.float32) + head_pair).astype(jnp.bfloat16)
        resid_full = x_gather(resid_pair)
        resid_part = lax.dynamic_slice_in_dim(
            resid_pair, (lax.axis_index("tp") % 2) * width, width, 1
        )
        resid_full = after(resid_full, "lifted", lead)
        normed_mlp = rms_normed(resid_full.astype(jnp.float32), mlp_gain)
        gate = jnp.dot(normed_mlp, w_gate, preferred_element_type=jnp.float32)
        lift = jnp.dot(normed_mlp, w_up, preferred_element_type=jnp.float32)
        hidden = (jax.nn.silu(gate) * lift).astype(jnp.bfloat16)
        down_term = jnp.dot(hidden, w_down, preferred_element_type=jnp.float32)
        marks["lifted"] = down_term
        down_part = tp_reduce(down_term.astype(jnp.bfloat16))
        return (resid_part.astype(jnp.float32) + down_part).astype(jnp.bfloat16), marks

    first_out, first_marks = denoise(x_part[:block])
    second_in = after(x_part[block:], "gathered", first_marks)
    second_out, _ = denoise(second_in, first_marks)
    return (first_out, second_out)


def solution(mesh):
    placed = (
        P(GRP),
        P(GRP),
        P(GRP),
        P(),
        P(),
        P(GRP, "tp"),
        P(),
        P(None, "tp"),
        P(None, "tp"),
        P(None, "tp"),
        P("tp", None),
        P(),
        P(None, "tp"),
        P(None, "tp"),
        P("tp", None),
        P(GRP, "tp"),
        P(GRP, "tp"),
    )
    return jax.shard_map(
        on_device,
        mesh=mesh,
        in_specs=placed,
        out_specs=(P(GRP, "tp"), P(GRP, "tp")),
        check_vma=False,
    )
```

```python
import jax
import jax.numpy as jnp
from jax import lax
from jax.sharding import PartitionSpec as P
from jax.experimental import pallas as pl
from jax.experimental.pallas import tpu as pltpu

HD = 64
GRP = "grp"


EPSILON = 1e-05
SENTINEL = -1e30


def shifted(array, axis, step):
    n = lax.axis_size(axis)
    return lax.ppermute(array, axis, [(i, (i + step) % n) for i in range(n)])


def swapped(array, axis, bit):
    return lax.ppermute(array, axis, [(i, i ^ 1 << bit) for i in range(lax.axis_size(axis))])


def rolled(array, axis, shift):
    n = array.shape[axis]
    doubled = jnp.concatenate([array, array], axis=axis)
    return lax.dynamic_slice_in_dim(doubled, shift, n, axis)


def x_gather(pair):
    n_x = lax.axis_size("tp") // 2
    got = [pair] + [shifted(pair, "tp", 2 * k) for k in range(1, n_x)]
    return jnp.concatenate([got[-j % n_x] for j in range(n_x)], axis=1)


def tp_gather(part):
    me = lax.axis_index("tp")
    partner = swapped(part, "tp", 0)
    pair = jnp.where(
        me % 2 == 0,
        jnp.concatenate([part, partner], axis=1),
        jnp.concatenate([partner, part], axis=1),
    )
    return x_gather(pair)


def x_reduce(full):
    rows, total_width = full.shape
    n_x = lax.axis_size("tp") // 2
    span = total_width // n_x
    acc = full[:, :span].astype(jnp.float32)
    for k in range(1, n_x):
        piece = full[:, k * span : (k + 1) * span]
        acc = acc + shifted(piece, "tp", 2 * k).astype(jnp.float32)
    return acc


def tp_reduce(full):
    me = lax.axis_index("tp")
    acc = x_reduce(full)
    rows, span = acc.shape
    halves = acc.reshape(rows, 2, span // 2)
    low = me % 2 == 0
    mine = jnp.where(low, halves[:, 0], halves[:, 1])
    other = jnp.where(low, halves[:, 1], halves[:, 0])
    got = swapped(other.astype(jnp.bfloat16), "tp", 0)
    return mine + got.astype(jnp.float32)


def pair_reduce(full):
    rounded = x_reduce(full).astype(jnp.bfloat16)
    return rounded.astype(jnp.float32) + swapped(rounded, "tp", 0).astype(jnp.float32)


def rms_normed(values, gain):
    square = jnp.mean(values * values, axis=-1, keepdims=True)
    return (values * lax.rsqrt(square + EPSILON) * gain).astype(jnp.bfloat16)


def rotate(vectors, positions):
    half = vectors.shape[-1] // 2
    exponent = jnp.arange(half, dtype=jnp.float32) * (-2.0 / vectors.shape[-1])
    freqs = jnp.power(jnp.float32(10000.0), exponent)
    angles = positions.astype(jnp.float32)[:, None] * freqs[None, :]
    cosine = jnp.cos(angles)[:, None, :]
    sine = jnp.sin(angles)[:, None, :]
    first = vectors[..., :half]
    second = vectors[..., half:]
    return jnp.concatenate(
        [first * cosine - second * sine, second * cosine + first * sine], axis=-1
    )


def attention_kernel(q_ref, ko_ref, kf_ref, kn_ref, vo_ref, vf_ref, vn_ref, mo_ref, mf_ref, o_ref):
    query = q_ref[0]
    contract = (((1,), (1,)), ((), ()))
    parts = []
    for keys, bias in ((ko_ref[...], mo_ref[...]), (kf_ref[...], mf_ref[...]), (kn_ref[0], None)):
        scores = lax.dot_general(query, keys, contract, preferred_element_type=jnp.float32)
        if bias is not None:
            scores = scores + bias
        parts.append(scores)
    top = parts[0].max(axis=-1, keepdims=True)
    for scores in parts[1:]:
        top = jnp.maximum(top, scores.max(axis=-1, keepdims=True))
    total = jnp.zeros_like(top)
    weighted = jnp.zeros((query.shape[0], vn_ref.shape[-1]), jnp.float32)
    for scores, values in zip(parts, (vo_ref[...], vf_ref[...], vn_ref[0])):
        weights = jnp.exp(scores - top)
        total = total + weights.sum(axis=-1, keepdims=True)
        weighted = weighted + jnp.dot(
            weights.astype(jnp.bfloat16), values, preferred_element_type=jnp.float32
        )
    o_ref[0] = (weighted / total).astype(o_ref.dtype)


def attention(query, own_keys, far_keys, new_keys, own_values, far_values, new_values, own_mask, far_mask):
    passes, rows, depth = query.shape
    tile = 256
    n_own = own_keys.shape[0]
    n_far = far_keys.shape[0]
    n_new = new_keys.shape[1]
    n_keys = n_own + n_far + n_new
    whole = lambda shape: pl.BlockSpec(shape, lambda p, i: (0,) * len(shape))
    per_pass = pl.BlockSpec((1, n_new, depth), lambda p, i: (p, 0, 0))
    return pl.pallas_call(
        attention_kernel,
        grid=(passes, rows // tile),
        in_specs=[
            pl.BlockSpec((1, tile, depth), lambda p, i: (p, i, 0)),
            whole((n_own, depth)),
            whole((n_far, depth)),
            per_pass,
            whole((n_own, depth)),
            whole((n_far, depth)),
            per_pass,
            whole((1, n_own)),
            whole((1, n_far)),
        ],
        out_specs=pl.BlockSpec((1, tile, depth), lambda p, i: (p, i, 0)),
        out_shape=jax.ShapeDtypeStruct(query.shape, jnp.bfloat16),
        cost_estimate=pl.CostEstimate(
            flops=4 * passes * rows * n_keys * depth,
            transcendentals=passes * rows * n_keys,
            bytes_accessed=2 * (2 * passes * rows * depth + 2 * n_keys * depth),
        ),
    )(query, own_keys, far_keys, new_keys, own_values, far_values, new_values, own_mask, far_mask)


def on_device(
    tok_ids,
    accept,
    sub_ids,
    cache_len,
    spill,
    embed,
    attn_gain,
    w_query,
    w_key,
    w_value,
    w_out,
    mlp_gain,
    w_gate,
    w_up,
    w_down,
    cache_keys,
    cache_values,
):
    block = tok_ids.shape[0]
    slots = cache_keys.shape[0]
    query_local = w_query.shape[1] // HD
    stored_local = w_key.shape[1] // HD
    per_stored = query_local // stored_local
    group_index = lax.axis_index(GRP)
    own_count = cache_len[group_index] - spill[group_index]
    far_count = spill[group_index]
    positions = cache_len[group_index] + jnp.arange(block, dtype=jnp.int32)
    slot_ids = jnp.arange(slots, dtype=jnp.int32)
    tail_ids = slot_ids[block:]
    store_keys = cache_keys.reshape(slots, stored_local, HD)
    store_values = cache_values.reshape(slots, stored_local, HD)
    second_ids = jnp.where(accept == 1, sub_ids, tok_ids)

    table = lax.all_gather(embed, GRP, axis=0, tiled=True)
    first_part = jnp.take(table, tok_ids, axis=0)
    rows, width = first_part.shape

    tails = swapped(jnp.concatenate([cache_keys[block:], cache_values[block:]], axis=1), GRP, 0)
    tail_keys, tail_values = jnp.split(tails, 2, axis=1)
    far_keys = tail_keys.reshape(slots - block, stored_local, HD)
    far_values = tail_values.reshape(slots - block, stored_local, HD)
    far_valid = tail_ids >= slots - far_count
    own_valid = slot_ids < own_count

    own_mask = jnp.where(own_valid, 0.0, SENTINEL)[None]
    far_mask = jnp.where(far_valid, 0.0, SENTINEL)[None]
    mine_x = lax.axis_index("tp") // 2
    shift = mine_x * 2 * width
    attn_gain = rolled(attn_gain, 0, shift)
    mlp_gain = rolled(mlp_gain, 0, shift)
    w_query = rolled(w_query, 0, shift)
    w_key = rolled(w_key, 0, shift)
    w_value = rolled(w_value, 0, shift)
    w_gate = rolled(w_gate, 0, shift)
    w_up = rolled(w_up, 0, shift)
    w_out = rolled(w_out, 1, shift)
    w_down = rolled(w_down, 1, shift)

    def after(value, stage, lead):
        if lead is None:
            return value
        return lax.optimization_barrier((value, lead[stage]))[0]

    def denoise(x_part, lead=None):
        marks = {}
        x_full = tp_gather(x_part)
        marks["gathered"] = x_full
        x_full = after(x_full, "attended", lead)
        normed = rms_normed(x_full.astype(jnp.float32), attn_gain)
        query = (
            rotate(
                jnp.dot(normed, w_query, preferred_element_type=jnp.float32).reshape(
                    block, query_local, HD
                ),
                positions,
            )
            * 0.125
        ).astype(jnp.bfloat16)
        new_keys = rotate(
            jnp.dot(normed, w_key, preferred_element_type=jnp.float32).reshape(
                block, stored_local, HD
            ),
            positions,
        ).astype(jnp.bfloat16)
        new_values = jnp.dot(normed, w_value, preferred_element_type=jnp.float32).astype(
            jnp.bfloat16
        )
        mixed_heads = attention(
            query.reshape(1, block * per_stored, HD),
            store_keys.reshape(slots, HD),
            far_keys.reshape(slots - block, HD),
            new_keys.reshape(1, block, HD),
            store_values.reshape(slots, HD),
            far_values.reshape(slots - block, HD),
            new_values.reshape(1, block, HD),
            own_mask,
            far_mask,
        )
        mixed = mixed_heads.reshape(block, query_local * HD)
        head_term = jnp.dot(mixed, w_out, preferred_element_type=jnp.float32)
        marks["attended"] = head_term
        head_pair = pair_reduce(head_term.astype(jnp.bfloat16))
        span = head_pair.shape[1]
        x_pair = x_full[:, :span]
        resid_pair = (x_pair.astype(jnp.float32) + head_pair).astype(jnp.bfloat16)
        resid_full = x_gather(resid_pair)
        resid_part = lax.dynamic_slice_in_dim(
            resid_pair, (lax.axis_index("tp") % 2) * width, width, 1
        )
        resid_full = after(resid_full, "lifted", lead)
        normed_mlp = rms_normed(resid_full.astype(jnp.float32), mlp_gain)
        gate = jnp.dot(normed_mlp, w_gate, preferred_element_type=jnp.float32)
        lift = jnp.dot(normed_mlp, w_up, preferred_element_type=jnp.float32)
        hidden = (jax.nn.silu(gate) * lift).astype(jnp.bfloat16)
        down_term = jnp.dot(hidden, w_down, preferred_element_type=jnp.float32)
        marks["lifted"] = down_term
        down_part = tp_reduce(down_term.astype(jnp.bfloat16))
        return (resid_part.astype(jnp.float32) + down_part).astype(jnp.bfloat16), marks

    first_out, first_marks = denoise(first_part)
    second_in = after(jnp.take(table, second_ids, axis=0), "gathered", first_marks)
    second_out, _ = denoise(second_in, first_marks)
    return (first_out, second_out)


def solution(mesh):
    placed = (
        P(GRP),
        P(GRP),
        P(GRP),
        P(),
        P(),
        P(GRP, "tp"),
        P(),
        P(None, "tp"),
        P(None, "tp"),
        P(None, "tp"),
        P("tp", None),
        P(),
        P(None, "tp"),
        P(None, "tp"),
        P("tp", None),
        P(GRP, "tp"),
        P(GRP, "tp"),
    )
    return jax.shard_map(
        on_device,
        mesh=mesh,
        in_specs=placed,
        out_specs=(P(GRP, "tp"), P(GRP, "tp")),
        check_vma=False,
    )
```

```python
import jax
import jax.numpy as jnp
from jax import lax
from jax.sharding import PartitionSpec as P
from jax.experimental import pallas as pl
from jax.experimental.pallas import tpu as pltpu

HD = 64
GRP = "grp"


EPSILON = 1e-05
SENTINEL = -1e30


def shifted(array, axis, step):
    n = lax.axis_size(axis)
    return lax.ppermute(array, axis, [(i, (i + step) % n) for i in range(n)])


def swapped(array, axis, bit):
    return lax.ppermute(array, axis, [(i, i ^ 1 << bit) for i in range(lax.axis_size(axis))])


def rolled(array, axis, shift):
    n = array.shape[axis]
    doubled = jnp.concatenate([array, array], axis=axis)
    return lax.dynamic_slice_in_dim(doubled, shift, n, axis)


def x_gather(pair):
    n_x = lax.axis_size("tp") // 2
    got = [pair] + [shifted(pair, "tp", 2 * k) for k in range(1, n_x)]
    return jnp.concatenate([got[-j % n_x] for j in range(n_x)], axis=1)


def tp_gather(part):
    me = lax.axis_index("tp")
    partner = swapped(part, "tp", 0)
    pair = jnp.where(
        me % 2 == 0,
        jnp.concatenate([part, partner], axis=1),
        jnp.concatenate([partner, part], axis=1),
    )
    return x_gather(pair)


def x_reduce(full):
    rows, total_width = full.shape
    n_x = lax.axis_size("tp") // 2
    span = total_width // n_x
    acc = full[:, :span].astype(jnp.float32)
    for k in range(1, n_x):
        piece = full[:, k * span : (k + 1) * span]
        acc = acc + shifted(piece, "tp", 2 * k).astype(jnp.float32)
    return acc


def tp_reduce(full):
    me = lax.axis_index("tp")
    acc = x_reduce(full)
    rows, span = acc.shape
    halves = acc.reshape(rows, 2, span // 2)
    low = me % 2 == 0
    mine = jnp.where(low, halves[:, 0], halves[:, 1])
    other = jnp.where(low, halves[:, 1], halves[:, 0])
    got = swapped(other.astype(jnp.bfloat16), "tp", 0)
    return mine + got.astype(jnp.float32)


def pair_reduce(full):
    rounded = x_reduce(full).astype(jnp.bfloat16)
    return rounded.astype(jnp.float32) + swapped(rounded, "tp", 0).astype(jnp.float32)


def rms_normed(values, gain):
    square = jnp.mean(values * values, axis=-1, keepdims=True)
    return (values * lax.rsqrt(square + EPSILON) * gain).astype(jnp.bfloat16)


def rotate(vectors, positions):
    half = vectors.shape[-1] // 2
    exponent = jnp.arange(half, dtype=jnp.float32) * (-2.0 / vectors.shape[-1])
    freqs = jnp.power(jnp.float32(10000.0), exponent)
    angles = positions.astype(jnp.float32)[:, None] * freqs[None, :]
    cosine = jnp.cos(angles)[:, None, :]
    sine = jnp.sin(angles)[:, None, :]
    first = vectors[..., :half]
    second = vectors[..., half:]
    return jnp.concatenate(
        [first * cosine - second * sine, second * cosine + first * sine], axis=-1
    )


def attention_kernel(q_ref, ko_ref, kf_ref, kn_ref, vo_ref, vf_ref, vn_ref, mo_ref, mf_ref, o_ref):
    query = q_ref[0]
    contract = (((1,), (1,)), ((), ()))
    parts = []
    for keys, bias in ((ko_ref[...], mo_ref[...]), (kf_ref[...], mf_ref[...]), (kn_ref[0], None)):
        scores = lax.dot_general(query, keys, contract, preferred_element_type=jnp.float32)
        if bias is not None:
            scores = scores + bias
        parts.append(scores)
    top = parts[0].max(axis=-1, keepdims=True)
    for scores in parts[1:]:
        top = jnp.maximum(top, scores.max(axis=-1, keepdims=True))
    total = jnp.zeros_like(top)
    weighted = jnp.zeros((query.shape[0], vn_ref.shape[-1]), jnp.float32)
    for scores, values in zip(parts, (vo_ref[...], vf_ref[...], vn_ref[0])):
        weights = jnp.exp(scores - top)
        total = total + weights.sum(axis=-1, keepdims=True)
        weighted = weighted + jnp.dot(
            weights.astype(jnp.bfloat16), values, preferred_element_type=jnp.float32
        )
    o_ref[0] = (weighted / total).astype(o_ref.dtype)


def attention(query, own_keys, far_keys, new_keys, own_values, far_values, new_values, own_mask, far_mask):
    passes, rows, depth = query.shape
    tile = 256
    n_own = own_keys.shape[0]
    n_far = far_keys.shape[0]
    n_new = new_keys.shape[1]
    n_keys = n_own + n_far + n_new
    whole = lambda shape: pl.BlockSpec(shape, lambda p, i: (0,) * len(shape))
    per_pass = pl.BlockSpec((1, n_new, depth), lambda p, i: (p, 0, 0))
    return pl.pallas_call(
        attention_kernel,
        grid=(passes, rows // tile),
        in_specs=[
            pl.BlockSpec((1, tile, depth), lambda p, i: (p, i, 0)),
            whole((n_own, depth)),
            whole((n_far, depth)),
            per_pass,
            whole((n_own, depth)),
            whole((n_far, depth)),
            per_pass,
            whole((1, n_own)),
            whole((1, n_far)),
        ],
        out_specs=pl.BlockSpec((1, tile, depth), lambda p, i: (p, i, 0)),
        out_shape=jax.ShapeDtypeStruct(query.shape, jnp.bfloat16),
        cost_estimate=pl.CostEstimate(
            flops=4 * passes * rows * n_keys * depth,
            transcendentals=passes * rows * n_keys,
            bytes_accessed=2 * (2 * passes * rows * depth + 2 * n_keys * depth),
        ),
    )(query, own_keys, far_keys, new_keys, own_values, far_values, new_values, own_mask, far_mask)


def on_device(
    tok_ids,
    accept,
    sub_ids,
    cache_len,
    spill,
    embed,
    attn_gain,
    w_query,
    w_key,
    w_value,
    w_out,
    mlp_gain,
    w_gate,
    w_up,
    w_down,
    cache_keys,
    cache_values,
):
    block = tok_ids.shape[0]
    slots = cache_keys.shape[0]
    query_local = w_query.shape[1] // HD
    stored_local = w_key.shape[1] // HD
    per_stored = query_local // stored_local
    group_index = lax.axis_index(GRP)
    own_count = cache_len[group_index] - spill[group_index]
    far_count = spill[group_index]
    positions = cache_len[group_index] + jnp.arange(block, dtype=jnp.int32)
    slot_ids = jnp.arange(slots, dtype=jnp.int32)
    tail_ids = slot_ids[block:]
    store_keys = cache_keys.reshape(slots, stored_local, HD)
    store_values = cache_values.reshape(slots, stored_local, HD)
    second_ids = jnp.where(accept == 1, sub_ids, tok_ids)

    table = lax.all_gather(embed, GRP, axis=0, tiled=True)
    first_part = jnp.take(table, tok_ids, axis=0)
    rows, width = first_part.shape

    tails = swapped(jnp.concatenate([cache_keys[block:], cache_values[block:]], axis=1), GRP, 0)
    tail_keys, tail_values = jnp.split(tails, 2, axis=1)
    far_keys = tail_keys.reshape(slots - block, stored_local, HD)
    far_values = tail_values.reshape(slots - block, stored_local, HD)
    far_valid = tail_ids >= slots - far_count
    own_valid = slot_ids < own_count

    own_mask = jnp.where(own_valid, 0.0, SENTINEL)[None]
    far_mask = jnp.where(far_valid, 0.0, SENTINEL)[None]
    mine_x = lax.axis_index("tp") // 2
    shift = mine_x * 2 * width
    attn_gain = rolled(attn_gain, 0, shift)
    mlp_gain = rolled(mlp_gain, 0, shift)
    w_query = rolled(w_query, 0, shift)
    w_key = rolled(w_key, 0, shift)
    w_value = rolled(w_value, 0, shift)
    w_gate = rolled(w_gate, 0, shift)
    w_up = rolled(w_up, 0, shift)
    w_out = rolled(w_out, 1, shift)
    w_down = rolled(w_down, 1, shift)

    def after(value, stage, lead):
        if lead is None:
            return value
        return lax.optimization_barrier((value, lead[stage]))[0]

    def denoise(x_part, lead=None):
        marks = {}
        x_full = tp_gather(x_part)
        marks["gathered"] = x_full
        normed = rms_normed(x_full.astype(jnp.float32), attn_gain)
        query = (
            rotate(
                jnp.dot(normed, w_query, preferred_element_type=jnp.float32).reshape(
                    block, query_local, HD
                ),
                positions,
            )
            * 0.125
        ).astype(jnp.bfloat16)
        new_keys = rotate(
            jnp.dot(normed, w_key, preferred_element_type=jnp.float32).reshape(
                block, stored_local, HD
            ),
            positions,
        ).astype(jnp.bfloat16)
        new_values = jnp.dot(normed, w_value, preferred_element_type=jnp.float32).astype(
            jnp.bfloat16
        )
        mixed_heads = attention(
            query.reshape(1, block * per_stored, HD),
            store_keys.reshape(slots, HD),
            far_keys.reshape(slots - block, HD),
            new_keys.reshape(1, block, HD),
            store_values.reshape(slots, HD),
            far_values.reshape(slots - block, HD),
            new_values.reshape(1, block, HD),
            own_mask,
            far_mask,
        )
        mixed = mixed_heads.reshape(block, query_local * HD)
        head_term = jnp.dot(mixed, w_out, preferred_element_type=jnp.float32)
        marks["attended"] = head_term
        head_pair = pair_reduce(head_term.astype(jnp.bfloat16))
        span = head_pair.shape[1]
        x_pair = x_full[:, :span]
        resid_pair = (x_pair.astype(jnp.float32) + head_pair).astype(jnp.bfloat16)
        resid_full = x_gather(resid_pair)
        resid_part = lax.dynamic_slice_in_dim(
            resid_pair, (lax.axis_index("tp") % 2) * width, width, 1
        )
        normed_mlp = rms_normed(resid_full.astype(jnp.float32), mlp_gain)
        gate = jnp.dot(normed_mlp, w_gate, preferred_element_type=jnp.float32)
        lift = jnp.dot(normed_mlp, w_up, preferred_element_type=jnp.float32)
        hidden = (jax.nn.silu(gate) * lift).astype(jnp.bfloat16)
        down_term = jnp.dot(hidden, w_down, preferred_element_type=jnp.float32)
        marks["lifted"] = down_term
        down_part = tp_reduce(down_term.astype(jnp.bfloat16))
        return (resid_part.astype(jnp.float32) + down_part).astype(jnp.bfloat16), marks

    first_out, first_marks = denoise(first_part)
    second_in = jnp.take(table, second_ids, axis=0)
    second_out, _ = denoise(second_in, first_marks)
    return (first_out, second_out)


def solution(mesh):
    placed = (
        P(GRP),
        P(GRP),
        P(GRP),
        P(),
        P(),
        P(GRP, "tp"),
        P(),
        P(None, "tp"),
        P(None, "tp"),
        P(None, "tp"),
        P("tp", None),
        P(),
        P(None, "tp"),
        P(None, "tp"),
        P("tp", None),
        P(GRP, "tp"),
        P(GRP, "tp"),
    )
    return jax.shard_map(
        on_device,
        mesh=mesh,
        in_specs=placed,
        out_specs=(P(GRP, "tp"), P(GRP, "tp")),
        check_vma=False,
    )
```
